512 devices in a mesh: expert: 128 (over x, z, core), dp: 4 (over y).
Axes of the slice: x: 4, y: 4, z: 16, core: 2. Of those that a mesh axis runs over, the one named last changes fastest.
Arguments:
- tokens: bfloat16 [16384, 3584], P('expert', 'dp'), may hold values from -6 to 6
- routes: int32 [16384, 2], P('expert'), may hold values from 0 to 63, all different within a row; in each aligned block of 128 rows (0 to 127, 128 to 255, ...) at most 6 rows name the same one
- logits: float32 [16384, 2], P('expert'), may hold values from -6 to 6
- cotangent: bfloat16 [16384, 3584], P('expert', 'dp'), may hold values from -6 to 6
- pair_flags: int32 [32], replicated, may hold values from -1000 to 999
- w_up: bfloat16 [3584, 65536], P('dp', 'expert'), may hold values from -0.09375 to 0.09375
- w_down: bfloat16 [3584, 65536], P('dp', 'expert'), may hold values from -0.1875 to 0.1875
Outputs:
- grad_tokens: bfloat16 [16384, 3584], P('expert', 'dp')
- grad_logits: float32 [16384, 2], P('expert')
- grad_up: bfloat16 [3584, 65536], P('dp', 'expert')
- grad_down: bfloat16 [3584, 65536], P('dp', 'expert')
The draws below stay inside these ranges and needn't reach their ends.
Inputs may be any that keep to these rules, and one draw needn't show every extreme that they name: `routes`: among the 128 tokens of one index of the expert axis no expert is named more than 6 times, a bound that some block reaches; a token names 2 distinct experts.
All inputs are finite; a program needn't handle non-finite values.
Results may differ from the reference program's by a relative error of at most 0.02.
Values may be sent and summed in bfloat16 or wider, within the bound.
No kernel may reach another device: no remote copies, remote signals or barrier semaphores. Data moves between devices by JAX's collectives and lax.ppermute only.
A program may use at most 64 MiB of HBM per device.

```python
import math
import jax
import jax.numpy as jnp
import numpy as np
from jax import lax

D = 3584
FF = 1024
TOPK = 2
TOK_DEV = 128
EXPERTS = 64
HALF = 32
CAP = 6
TOKENS = 16384
N_EXPERT = 128


def plant(drawn, key, smallest, largest):
    extent = drawn.shape
    index_at = [jax.random.randint(jax.random.fold_in(key, axis), (), 0, extent[axis]) for axis in range(len(extent))]
    drawn = drawn.at[tuple(index_at)].set(smallest)
    longest = extent.index(max(extent))
    index_at[longest] = (index_at[longest] + 1) % extent[longest]
    return drawn.at[tuple(index_at)].set(largest)


def block_scale(own_key, shape, pieces, least, top_value):
    def one(axis_at, parts):
        draws = jax.random.uniform(jax.random.fold_in(jax.random.fold_in(own_key, 6), axis_at), (parts,), jnp.float32, least / len(pieces), top_value / len(pieces))
        return jnp.repeat(jnp.exp(draws), shape[axis_at] // parts).reshape((-1,) + (1,) * (len(shape) - axis_at - 1))

    loudness = one(*pieces[0])
    for cut in pieces[1:]:
        loudness = loudness * one(*cut)
    return loudness


def deal_out(key, own, number, rows, count, top, reach, lean):
    ranking = jax.random.permutation(key, count)
    crowded, usual = load_shares(count, rows * top, reach, lean, True), load_shares(count, rows * top, reach, lean, False)
    places = jnp.arange(count)

    def named(sizes, turn):
        used = int((sizes > 0).sum())
        fixed = max(1, used // 4)
        passed = fixed + (places - fixed + turn * (used - fixed)) % max(1, count - fixed)
        return jnp.zeros((count,), jnp.int32).at[ranking[jnp.where(places < fixed, places, passed)]].set(jnp.asarray(sizes, jnp.int32))

    sizes = jnp.where(number % 4 == 0, named(crowded, number // 4), named(usual, number - number // 4 - 1))
    mixed = jax.random.permutation(jax.random.fold_in(own, 3), count)
    donor, taker = mixed[0:count // 2 * 2:2], mixed[1:count // 2 * 2:2]
    margin = jnp.minimum(sizes[donor] - 1, reach - sizes[taker]) // 2
    margin = jnp.where((donor == ranking[0]) | (taker == ranking[0]) | (sizes[taker] == 0), 0, jnp.maximum(margin, 0))
    passed = jax.random.randint(jax.random.fold_in(own, 4), (count // 2,), 0, 1 << 20) % (margin + 1)
    sizes = sizes.at[donor].add(-passed).at[taker].add(passed)
    members = jnp.searchsorted(jnp.cumsum(sizes), jnp.arange(rows * top), side="right").astype(jnp.int32)
    table = members.reshape(top, rows).T
    table = table[jax.random.permutation(jax.random.fold_in(own, 1), rows)]
    turn = jax.random.randint(jax.random.fold_in(own, 2), (rows, 1), 0, top)
    return jnp.take_along_axis(table, (jnp.arange(top)[None, :] + turn) % top, axis=1)


def load_shares(count, total, limit, lean, full):
    loads = [(1 << 20) // math.isqrt(rank ** lean) + 1 for rank in range(1, count + 1)]
    largest = limit if full else min(limit, max(-(-total // count), total * loads[0] // sum(loads)))
    least = 1 if total - largest >= count - 1 else 0
    counts, rest = [largest] + [least] * (count - 1), total - largest - least * (count - 1)
    while rest > 0:
        candidates = [i for i in range(1, count) if counts[i] < largest] or [i for i in range(1, count) if counts[i] < limit]
        mass, left = sum([loads[i] for i in candidates]), rest
        for i in candidates:
            extra = min(limit - counts[i], max(1, left * loads[i] // mass), rest)
            counts[i] = counts[i] + extra
            rest = rest - extra
    return np.array(counts)


def scatter_about(own_key, shape, spread, reach, split=(), held_as=jnp.bfloat16):
    result = spread * jax.random.normal(own_key, shape, jnp.float32)
    if split:
        result = result * block_scale(own_key, shape, split, -0.22, 0.18)
    return jnp.clip(result, -reach, reach).astype(held_as)


def setup_inputs(seed: int = 0) -> dict:
    splits = jax.random.split(jax.random.key(seed), 8)
    tokens = scatter_about(splits[0], (TOKENS, D), 1.0, 6.0, ((0, 128), (1, 4)))
    routes_keys = jax.random.split(jax.random.fold_in(splits[1], 1), TOKENS // TOK_DEV)
    routes_turns = jax.random.permutation(jax.random.fold_in(splits[1], 3), TOKENS // TOK_DEV)
    routes = jax.vmap(lambda own, number: deal_out(jax.random.fold_in(splits[1], 2), own, number, TOK_DEV, EXPERTS, TOPK, CAP, 2))(routes_keys, routes_turns).reshape((TOKENS, TOPK))
    logits = scatter_about(splits[2], (TOKENS, TOPK), 2.0, 6.0, ((0, 128),), jnp.float32)
    cotangent = scatter_about(splits[3], (TOKENS, D), 1.0, 6.0, ((0, 128), (1, 4)))
    pair_flags = plant(jax.random.randint(splits[4], (HALF,), -1000, 1000), jax.random.fold_in(splits[4], 1), -1000, 999).astype(jnp.int32)
    w_up = scatter_about(splits[5], (D, EXPERTS * FF), D ** -0.5, 0.09375, ((0, 4), (1, 128)))
    w_down = scatter_about(splits[6], (D, EXPERTS * FF), FF ** -0.5, 0.1875, ((0, 4), (1, 128)))
    return dict(tokens=tokens, routes=routes, logits=logits, cotangent=cotangent, pair_flags=pair_flags, w_up=w_up, w_down=w_down)


def reference(tokens, routes, logits, cotangent, pair_flags, w_up, w_down):
    per_block = TOK_DEV * TOPK
    route_total = N_EXPERT * per_block
    half_width = FF // 2
    expert_ids = jnp.arange(EXPERTS, dtype=jnp.int32)
    paired = jnp.concatenate([pair_flags, pair_flags]) > 0
    owner_slot = jnp.where(paired, (expert_ids + HALF) % EXPERTS, expert_ids).astype(jnp.int32)
    affinity = jax.nn.sigmoid(logits)
    weights = affinity / jnp.sum(affinity, -1, keepdims=True)
    flat_weights = weights.reshape(-1)
    grouped = routes.reshape(N_EXPERT, per_block).astype(jnp.int32)
    onehot = (grouped[:, :, None] == expert_ids[None, None, :]).astype(jnp.int32)
    slot_rank = (jnp.sum(jnp.cumsum(onehot, 1) * onehot, -1) - 1).astype(jnp.int32)
    block_ids = jnp.broadcast_to(jnp.arange(N_EXPERT, dtype=jnp.int32)[:, None], (N_EXPERT, per_block))
    route_ids = jnp.arange(route_total, dtype=jnp.int32).reshape(N_EXPERT, per_block)
    slot_table = jnp.full((EXPERTS, N_EXPERT, CAP), route_total, jnp.int32).at[grouped, block_ids, slot_rank].set(route_ids)
    up_blocks = w_up.reshape(D, EXPERTS, FF).transpose(1, 0, 2)
    down_blocks = w_down.reshape(D, EXPERTS, FF).transpose(1, 0, 2)

    def one_expert(totals, expert_item):
        grad_acc, pair_acc = totals
        slot_rows, up_block, down_block = expert_item
        row_index = slot_rows.reshape(-1)
        filled = row_index < route_total
        safe_index = jnp.where(filled, row_index, 0)
        token_index = safe_index // TOPK
        x_rows = jnp.where(filled[:, None], tokens[token_index], jnp.zeros((), tokens.dtype))
        c_rows = (flat_weights[safe_index][:, None] * cotangent[token_index].astype(jnp.float32)).astype(jnp.bfloat16)
        c_rows = jnp.where(filled[:, None], c_rows, jnp.zeros((), jnp.bfloat16))
        up_pre = jnp.dot(x_rows, up_block, preferred_element_type=jnp.float32)
        up_sig = jax.nn.sigmoid(up_pre)
        hidden = (up_pre * up_sig).astype(jnp.bfloat16)
        grad_hidden = jnp.dot(c_rows, down_block, preferred_element_type=jnp.float32)
        pair_halves = jnp.sum((hidden.astype(jnp.float32) * grad_hidden).reshape(-1, 2, half_width), -1).astype(jnp.bfloat16)
        grad_pre = (grad_hidden * up_sig * (1.0 + up_pre * (1.0 - up_sig))).astype(jnp.bfloat16)
        route_halves = jnp.einsum('nhf,dhf->nhd', grad_pre.astype(jnp.float32).reshape(-1, 2, half_width), up_block.astype(jnp.float32).reshape(D, 2, half_width)).astype(jnp.bfloat16)
        route_sum = jnp.sum(route_halves.astype(jnp.float32), 1)
        grad_up_e = jnp.dot(x_rows.T, grad_pre, preferred_element_type=jnp.float32).astype(jnp.bfloat16)
        grad_down_e = jnp.dot(c_rows.T, hidden, preferred_element_type=jnp.float32).astype(jnp.bfloat16)
        token_target = jnp.where(filled, token_index, TOKENS)
        grad_acc = grad_acc.at[token_target].add(route_sum, mode="drop")
        pair_target = jnp.where(filled, row_index, route_total)
        pair_acc = pair_acc.at[pair_target].set(jnp.sum(pair_halves.astype(jnp.float32), 1), mode="drop")
        return (grad_acc, pair_acc), (grad_up_e, grad_down_e)

    start = (jnp.zeros((TOKENS, D), jnp.float32), jnp.zeros((route_total,), jnp.float32))
    (grad_acc, pair_acc), (up_all, down_all) = lax.scan(one_expert, start, (slot_table, up_blocks, down_blocks))
    grad_tokens = grad_acc.astype(jnp.bfloat16)
    pairing_all = pair_acc.reshape(TOKENS, TOPK)
    grad_logits = (1.0 - affinity) * (pairing_all - weights * jnp.sum(pairing_all, -1, keepdims=True))
    grad_up = up_all[owner_slot].transpose(1, 0, 2).reshape(D, EXPERTS * FF)
    grad_down = down_all[owner_slot].transpose(1, 0, 2).reshape(D, EXPERTS * FF)
    return grad_tokens, grad_logits, grad_up, grad_down
```

```python
import jax
import jax.numpy as jnp
from jax import lax
from jax.sharding import PartitionSpec as P


def passed_along(value, axis, steps):
    count = lax.axis_size(axis)
    pairs = [(source, (source + steps) % count) for source in range(count)]
    return lax.ppermute(value, axis, pairs)


def core_swap(value, axis):
    count = lax.axis_size(axis)
    pairs = [(source, source ^ 1) for source in range(count)]
    return lax.ppermute(value, axis, pairs)


def pick_pair(swapped_here, theirs, ours):
    return tuple(
        (
            jnp.where(swapped_here, other_part, mine_part)
            for other_part, mine_part in zip(theirs, ours)
        )
    )


def activate(up_pre, grad_hidden):
    up_sig = jax.nn.sigmoid(up_pre)
    hidden = (up_pre * up_sig).astype(jnp.bfloat16)
    pairing_part = jnp.sum(hidden.astype(jnp.float32) * grad_hidden, -1)
    grad_pre = (grad_hidden * up_sig * (1.0 + up_pre * (1.0 - up_sig))).astype(jnp.bfloat16)
    return (hidden, pairing_part, grad_pre)


def local(tokens, routes, logits, cotangent, pair_flags, w_up, w_down):
    devices_ex = lax.axis_size("expert")
    experts = devices_ex // 2
    half_way = experts // 2
    here_index = lax.axis_index("expert")
    slot_here = here_index // 2
    first_core = (here_index % 2) == 0
    tok_rows, top_count = routes.shape
    quarter = tokens.shape[1]
    capacity = max(2, 2 * (3 * tok_rows * top_count // (4 * experts)))
    share = capacity // 2
    lanes = 128
    expert_ids = jnp.arange(experts, dtype=jnp.int32)
    paired = jnp.concatenate([pair_flags, pair_flags]) > 0
    owner_slot = jnp.where(paired, (expert_ids + half_way) % experts, expert_ids)
    swapped_here = paired[slot_here]
    affinity = jax.nn.sigmoid(logits)
    weights = affinity / jnp.sum(affinity, -1, keepdims=True)
    scaled = (weights[:, :, None] * cotangent[:, None, :].astype(jnp.float32)).astype(jnp.bfloat16)
    scaled = scaled.reshape(-1, quarter)
    flat_routes = routes.reshape(-1)
    onehot = (flat_routes[:, None] == expert_ids[None, :]).astype(jnp.int32)
    slot_rank = jnp.sum(jnp.cumsum(onehot, 0) * onehot, 1) - 1
    own_weights = (w_up, w_down)
    shifted = passed_along((w_up, w_down), "expert", devices_ex // 2)
    resident = pick_pair(swapped_here, shifted, own_weights)
    target = owner_slot[flat_routes]
    position = target * capacity + slot_rank
    empty_rows = jnp.zeros((experts * capacity, quarter), jnp.bfloat16)
    token_buf = (
        empty_rows.at[position]
        .set(jnp.repeat(tokens, top_count, axis=0))
        .reshape(experts, capacity, quarter)
    )
    scaled_buf = empty_rows.at[position].set(scaled).reshape(experts, capacity, quarter)
    dispatch = jnp.stack([token_buf, scaled_buf], axis=1).reshape(devices_ex, capacity, quarter)
    got = lax.all_to_all(dispatch, "expert", split_axis=0, concat_axis=0, tiled=True)
    partner_got = core_swap(got, "expert")
    routed_rows = jnp.where(first_core, got, partner_got).reshape(-1, quarter)
    scaled_rows = jnp.where(first_core, partner_got, got).reshape(-1, quarter)
    up_block, down_block = resident
    up_part = jnp.dot(routed_rows, up_block, preferred_element_type=jnp.float32)
    grad_part = jnp.dot(scaled_rows, down_block, preferred_element_type=jnp.float32)
    up_pre, grad_hidden = (
        lax.psum(up_part.astype(jnp.bfloat16), "dp").astype(jnp.float32),
        lax.psum(grad_part.astype(jnp.bfloat16), "dp").astype(jnp.float32),
    )
    hidden, pairing_part, grad_pre = activate(up_pre, grad_hidden)
    pairing_half = pairing_part.astype(jnp.bfloat16)
    route_half = jnp.einsum(
        "nf,df->nd", grad_pre, up_block, preferred_element_type=jnp.float32
    ).astype(jnp.bfloat16)
    grad_up = jnp.einsum(
        "nd,nf->df", routed_rows, grad_pre, preferred_element_type=jnp.float32
    ).astype(jnp.bfloat16)
    grad_down = jnp.einsum(
        "nd,nf->df", scaled_rows, hidden, preferred_element_type=jnp.float32
    ).astype(jnp.bfloat16)
    lane_ids = jnp.arange(lanes, dtype=jnp.int32)
    my_lane = jnp.where(first_core, 0, 1)
    pair_cols = jnp.where(
        lane_ids[None, None, :] == my_lane,
        pairing_half.reshape(devices_ex, capacity, 1),
        jnp.zeros((), jnp.bfloat16),
    )
    packed = jnp.concatenate(
        [route_half.reshape(devices_ex, capacity, quarter), pair_cols], axis=-1
    )
    low, high = packed[:, :share], packed[:, share:]
    keep = jnp.where(first_core, low, high)
    give = jnp.where(first_core, high, low)
    taken = core_swap(give, "expert")
    combined = (keep.astype(jnp.float32) + taken.astype(jnp.float32)).astype(jnp.bfloat16)
    back = lax.all_to_all(combined, "expert", split_axis=0, concat_axis=0, tiled=True)
    back_grid = back.reshape(experts, capacity, quarter + lanes)
    picked = back_grid[target, slot_rank]
    grad_tokens = jnp.sum(
        picked[:, :quarter].astype(jnp.float32).reshape(tok_rows, top_count, quarter), 1
    ).astype(jnp.bfloat16)
    pairing_mine = (
        picked[:, quarter].astype(jnp.float32) + picked[:, quarter + 1].astype(jnp.float32)
    ).reshape(tok_rows, top_count)
    grad_logits = (1.0 - affinity) * (
        pairing_mine - weights * jnp.sum(pairing_mine, -1, keepdims=True)
    )
    return (grad_tokens, grad_logits, grad_up, grad_down)


def solution(mesh):
    in_specs = (
        P("expert", "dp"),
        P("expert", None),
        P("expert", None),
        P("expert", "dp"),
        P(),
        P("dp", "expert"),
        P("dp", "expert"),
    )
    out_specs = (P("expert", "dp"), P("expert", None), P("dp", "expert"), P("dp", "expert"))
    return jax.shard_map(local, mesh=mesh, in_specs=in_specs, out_specs=out_specs, check_vma=False)
```

```python
import jax
import jax.numpy as jnp
from jax import lax
from jax.sharding import PartitionSpec as P


def passed_along(value, axis, steps):
    count = lax.axis_size(axis)
    pairs = [(source, (source + steps) % count) for source in range(count)]
    return lax.ppermute(value, axis, pairs)


def core_swap(value, axis):
    count = lax.axis_size(axis)
    pairs = [(source, source ^ 1) for source in range(count)]
    return lax.ppermute(value, axis, pairs)


def dp_sum(part, axis):
    count = lax.axis_size(axis)
    here = lax.axis_index(axis)
    rows = part.shape[0] // count
    blocks = part.reshape(count, rows, part.shape[1])
    total = blocks[here].astype(jnp.float32)
    for step in range(1, count):
        pairs = [(source, (source + step) % count) for source in range(count)]
        total = total + lax.ppermute(blocks[(here + step) % count], axis, pairs).astype(
            jnp.float32
        )
    reduced = total.astype(jnp.bfloat16)
    gathered = [reduced]
    for step in range(1, count):
        pairs = [(source, (source + step) % count) for source in range(count)]
        gathered.append(lax.ppermute(reduced, axis, pairs))
    stacked = jnp.stack(gathered)
    order = (here - jnp.arange(count)) % count
    return stacked[order].reshape(part.shape)


def pick_pair(swapped_here, theirs, ours):
    return tuple(
        (
            jnp.where(swapped_here, other_part, mine_part)
            for other_part, mine_part in zip(theirs, ours)
        )
    )


def activate(up_pre, grad_hidden):
    up_sig = jax.nn.sigmoid(up_pre)
    hidden = (up_pre * up_sig).astype(jnp.bfloat16)
    pairing_part = jnp.sum(hidden.astype(jnp.float32) * grad_hidden, -1)
    grad_pre = (grad_hidden * up_sig * (1.0 + up_pre * (1.0 - up_sig))).astype(jnp.bfloat16)
    return (hidden, pairing_part, grad_pre)


def layer(tokens, routes, logits, cotangent, pair_flags, w_up, w_down):
    devices_ex = lax.axis_size("expert")
    experts = devices_ex // 2
    half_way = experts // 2
    here_index = lax.axis_index("expert")
    slot_here = here_index // 2
    first_core = (here_index % 2) == 0
    tok_rows, top_count = routes.shape
    quarter = tokens.shape[1]
    capacity = max(2, 2 * (3 * tok_rows * top_count // (4 * experts)))
    share = capacity // 2
    lanes = 128
    expert_ids = jnp.arange(experts, dtype=jnp.int32)
    paired = jnp.concatenate([pair_flags, pair_flags]) > 0
    owner_slot = jnp.where(paired, (expert_ids + half_way) % experts, expert_ids)
    swapped_here = paired[slot_here]
    affinity = jax.nn.sigmoid(logits)
    weights = affinity / jnp.sum(affinity, -1, keepdims=True)
    scaled = (weights[:, :, None] * cotangent[:, None, :].astype(jnp.float32)).astype(jnp.bfloat16)
    scaled = scaled.reshape(-1, quarter)
    flat_routes = routes.reshape(-1)
    onehot = (flat_routes[:, None] == expert_ids[None, :]).astype(jnp.int32)
    slot_rank = jnp.sum(jnp.cumsum(onehot, 0) * onehot, 1) - 1
    own_weights = (w_up, w_down)
    shifted = passed_along((w_up, w_down), "expert", devices_ex // 2)
    resident = pick_pair(swapped_here, shifted, own_weights)
    target = owner_slot[flat_routes]
    position = target * capacity + slot_rank
    empty_rows = jnp.zeros((experts * capacity, quarter), jnp.bfloat16)
    token_buf = (
        empty_rows.at[position]
        .set(jnp.repeat(tokens, top_count, axis=0))
        .reshape(experts, capacity, quarter)
    )
    scaled_buf = empty_rows.at[position].set(scaled).reshape(experts, capacity, quarter)
    dispatch = jnp.stack([token_buf, scaled_buf], axis=1).reshape(devices_ex, capacity, quarter)
    got = lax.all_to_all(dispatch, "expert", split_axis=0, concat_axis=0, tiled=True)
    partner_got = core_swap(got, "expert")
    routed_rows = jnp.where(first_core, got, partner_got).reshape(-1, quarter)
    scaled_rows = jnp.where(first_core, partner_got, got).reshape(-1, quarter)
    up_block, down_block = resident
    up_part = jnp.dot(routed_rows, up_block, preferred_element_type=jnp.float32)
    grad_part = jnp.dot(scaled_rows, down_block, preferred_element_type=jnp.float32)
    width = up_part.shape[1]
    both = jnp.concatenate(
        [up_part.astype(jnp.bfloat16), grad_part.astype(jnp.bfloat16)], axis=1
    )
    summed = dp_sum(both, "dp").astype(jnp.float32)
    up_pre, grad_hidden = summed[:, :width], summed[:, width:]
    hidden, pairing_part, grad_pre = activate(up_pre, grad_hidden)
    pairing_half = pairing_part.astype(jnp.bfloat16)
    route_half = jnp.einsum(
        "nf,df->nd", grad_pre, up_block, preferred_element_type=jnp.float32
    ).astype(jnp.bfloat16)
    grad_up = jnp.einsum(
        "nd,nf->df", routed_rows, grad_pre, preferred_element_type=jnp.float32
    ).astype(jnp.bfloat16)
    grad_down = jnp.einsum(
        "nd,nf->df", scaled_rows, hidden, preferred_element_type=jnp.float32
    ).astype(jnp.bfloat16)
    lane_ids = jnp.arange(lanes, dtype=jnp.int32)
    my_lane = jnp.where(first_core, 0, 1)
    pair_cols = jnp.where(
        lane_ids[None, None, :] == my_lane,
        pairing_half.reshape(devices_ex, capacity, 1),
        jnp.zeros((), jnp.bfloat16),
    )
    packed = jnp.concatenate(
        [route_half.reshape(devices_ex, capacity, quarter), pair_cols], axis=-1
    )
    low, high = packed[:, :share], packed[:, share:]
    keep = jnp.where(first_core, low, high)
    give = jnp.where(first_core, high, low)
    taken = core_swap(give, "expert")
    combined = (keep.astype(jnp.float32) + taken.astype(jnp.float32)).astype(jnp.bfloat16)
    back = lax.all_to_all(combined, "expert", split_axis=0, concat_axis=0, tiled=True)
    back_grid = back.reshape(experts, capacity, quarter + lanes)
    picked = back_grid[target, slot_rank]
    grad_tokens = jnp.sum(
        picked[:, :quarter].astype(jnp.float32).reshape(tok_rows, top_count, quarter), 1
    ).astype(jnp.bfloat16)
    pairing_mine = (
        picked[:, quarter].astype(jnp.float32) + picked[:, quarter + 1].astype(jnp.float32)
    ).reshape(tok_rows, top_count)
    grad_logits = (1.0 - affinity) * (
        pairing_mine - weights * jnp.sum(pairing_mine, -1, keepdims=True)
    )
    return (grad_tokens, grad_logits, grad_up, grad_down)


def solution(mesh):
    in_specs = (
        P("expert", "dp"),
        P("expert", None),
        P("expert", None),
        P("expert", "dp"),
        P(),
        P("dp", "expert"),
        P("dp", "expert"),
    )
    out_specs = (P("expert", "dp"), P("expert", None), P("dp", "expert"), P("dp", "expert"))
    return jax.shard_map(layer, mesh=mesh, in_specs=in_specs, out_specs=out_specs, check_vma=False)
```

```python
import jax
import jax.numpy as jnp
from jax import lax
from jax.sharding import PartitionSpec as P


def passed_along(value, axis, steps):
    count = lax.axis_size(axis)
    pairs = [(source, (source + steps) % count) for source in range(count)]
    return lax.ppermute(value, axis, pairs)


def core_swap(value, axis):
    count = lax.axis_size(axis)
    pairs = [(source, source ^ 1) for source in range(count)]
    return lax.ppermute(value, axis, pairs)


def dp_sum(part, axis):
    count = lax.axis_size(axis)
    here = lax.axis_index(axis)
    rows = part.shape[0] // count
    blocks = part.reshape(count, rows, part.shape[1])
    total = blocks[here].astype(jnp.float32)
    for step in range(1, count):
        pairs = [(source, (source + step) % count) for source in range(count)]
        total = total + lax.ppermute(blocks[(here + step) % count], axis, pairs).astype(
            jnp.float32
        )
    reduced = total.astype(jnp.bfloat16)
    gathered = [reduced]
    for step in range(1, count):
        pairs = [(source, (source + step) % count) for source in range(count)]
        gathered.append(lax.ppermute(reduced, axis, pairs))
    stacked = jnp.stack(gathered)
    order = (here - jnp.arange(count)) % count
    return stacked[order].reshape(part.shape)


def lane_rows(value):
    count = value.shape[0]
    return value.reshape(count, -1, 128)


def pick_pair(swapped_here, theirs, ours):
    return tuple(
        (
            jnp.where(swapped_here, other_part, mine_part)
            for other_part, mine_part in zip(theirs, ours)
        )
    )


def activate(up_pre, grad_hidden):
    up_sig = jax.nn.sigmoid(up_pre)
    hidden = (up_pre * up_sig).astype(jnp.bfloat16)
    pairing_part = jnp.sum(hidden.astype(jnp.float32) * grad_hidden, -1)
    grad_pre = (grad_hidden * up_sig * (1.0 + up_pre * (1.0 - up_sig))).astype(jnp.bfloat16)
    return (hidden, pairing_part, grad_pre)


def layer(tokens, routes, logits, cotangent, pair_flags, w_up, w_down):
    devices_ex = lax.axis_size("expert")
    experts = devices_ex // 2
    half_way = experts // 2
    here_index = lax.axis_index("expert")
    slot_here = here_index // 2
    first_core = (here_index % 2) == 0
    tok_rows, top_count = routes.shape
    quarter = tokens.shape[1]
    capacity = max(2, 2 * (3 * tok_rows * top_count // (4 * experts)))
    share = capacity // 2
    lanes = 128
    expert_ids = jnp.arange(experts, dtype=jnp.int32)
    paired = jnp.concatenate([pair_flags, pair_flags]) > 0
    owner_slot = jnp.where(paired, (expert_ids + half_way) % experts, expert_ids)
    swapped_here = paired[slot_here]
    affinity = jax.nn.sigmoid(logits)
    weights = affinity / jnp.sum(affinity, -1, keepdims=True)
    scaled = (weights[:, :, None] * cotangent[:, None, :].astype(jnp.float32)).astype(jnp.bfloat16)
    scaled = scaled.reshape(-1, quarter)
    flat_routes = routes.reshape(-1)
    onehot = (flat_routes[:, None] == expert_ids[None, :]).astype(jnp.int32)
    slot_rank = jnp.sum(jnp.cumsum(onehot, 0) * onehot, 1) - 1
    own_weights = (w_up, w_down)
    shifted = passed_along((w_up, w_down), "expert", devices_ex // 2)
    resident = pick_pair(swapped_here, shifted, own_weights)
    target = owner_slot[flat_routes]
    position = target * capacity + slot_rank
    empty_rows = jnp.zeros((experts * capacity, quarter), jnp.bfloat16)
    token_buf = (
        empty_rows.at[position]
        .set(jnp.repeat(tokens, top_count, axis=0))
        .reshape(experts, capacity, quarter)
    )
    scaled_buf = empty_rows.at[position].set(scaled).reshape(experts, capacity, quarter)
    dispatch = jnp.stack([token_buf, scaled_buf], axis=1).reshape(devices_ex, capacity, quarter)
    got = lax.all_to_all(
        lane_rows(dispatch), "expert", split_axis=0, concat_axis=0, tiled=True
    ).reshape(devices_ex, capacity, quarter)
    partner_got = core_swap(got, "expert")
    routed_rows = jnp.where(first_core, got, partner_got).reshape(-1, quarter)
    scaled_rows = jnp.where(first_core, partner_got, got).reshape(-1, quarter)
    up_block, down_block = resident
    up_part = jnp.dot(routed_rows, up_block, preferred_element_type=jnp.float32)
    grad_part = jnp.dot(scaled_rows, down_block, preferred_element_type=jnp.float32)
    width = up_part.shape[1]
    both = jnp.concatenate(
        [up_part.astype(jnp.bfloat16), grad_part.astype(jnp.bfloat16)], axis=1
    )
    summed = dp_sum(both, "dp").astype(jnp.float32)
    up_pre, grad_hidden = summed[:, :width], summed[:, width:]
    hidden, pairing_part, grad_pre = activate(up_pre, grad_hidden)
    pairing_half = pairing_part.astype(jnp.bfloat16)
    route_half = jnp.einsum(
        "nf,df->nd", grad_pre, up_block, preferred_element_type=jnp.float32
    ).astype(jnp.bfloat16)
    grad_up = jnp.einsum(
        "nd,nf->df", routed_rows, grad_pre, preferred_element_type=jnp.float32
    ).astype(jnp.bfloat16)
    grad_down = jnp.einsum(
        "nd,nf->df", scaled_rows, hidden, preferred_element_type=jnp.float32
    ).astype(jnp.bfloat16)
    lane_ids = jnp.arange(lanes, dtype=jnp.int32)
    my_lane = jnp.where(first_core, 0, 1)
    pair_cols = jnp.where(
        lane_ids[None, None, :] == my_lane,
        pairing_half.reshape(devices_ex, capacity, 1),
        jnp.zeros((), jnp.bfloat16),
    )
    packed = jnp.concatenate(
        [route_half.reshape(devices_ex, capacity, quarter), pair_cols], axis=-1
    )
    low, high = packed[:, :share], packed[:, share:]
    keep = jnp.where(first_core, low, high)
    give = jnp.where(first_core, high, low)
    taken = core_swap(give, "expert")
    combined = (keep.astype(jnp.float32) + taken.astype(jnp.float32)).astype(jnp.bfloat16)
    back = lax.all_to_all(
        lane_rows(combined), "expert", split_axis=0, concat_axis=0, tiled=True
    )
    back_grid = back.reshape(experts, capacity, quarter + lanes)
    picked = back_grid[target, slot_rank]
    grad_tokens = jnp.sum(
        picked[:, :quarter].astype(jnp.float32).reshape(tok_rows, top_count, quarter), 1
    ).astype(jnp.bfloat16)
    pairing_mine = (
        picked[:, quarter].astype(jnp.float32) + picked[:, quarter + 1].astype(jnp.float32)
    ).reshape(tok_rows, top_count)
    grad_logits = (1.0 - affinity) * (
        pairing_mine - weights * jnp.sum(pairing_mine, -1, keepdims=True)
    )
    return (grad_tokens, grad_logits, grad_up, grad_down)


def solution(mesh):
    in_specs = (
        P("expert", "dp"),
        P("expert", None),
        P("expert", None),
        P("expert", "dp"),
        P(),
        P("dp", "expert"),
        P("dp", "expert"),
    )
    out_specs = (P("expert", "dp"), P("expert", None), P("dp", "expert"), P("dp", "expert"))
    return jax.shard_map(layer, mesh=mesh, in_specs=in_specs, out_specs=out_specs, check_vma=False)
```

```python
import jax
import jax.numpy as jnp
from jax import lax
from jax.sharding import PartitionSpec as P


def passed_along(value, axis, steps):
    count = lax.axis_size(axis)
    pairs = [(source, (source + steps) % count) for source in range(count)]
    return lax.ppermute(value, axis, pairs)


def core_swap(value, axis):
    count = lax.axis_size(axis)
    pairs = [(source, source ^ 1) for source in range(count)]
    return lax.ppermute(value, axis, pairs)


def dp_sum(part, axis):
    count = lax.axis_size(axis)
    rows = part.shape[0] // count
    blocks = lane_rows(part.reshape(count, rows, part.shape[1]))
    pieces = lax.all_to_all(blocks, axis, split_axis=0, concat_axis=0, tiled=True)
    reduced = jnp.sum(pieces.astype(jnp.float32), 0).astype(jnp.bfloat16)
    copies = jnp.broadcast_to(reduced[None], (count,) + reduced.shape)
    gathered = lax.all_to_all(copies, axis, split_axis=0, concat_axis=0, tiled=True)
    return gathered.reshape(part.shape)


def lane_rows(value):
    count = value.shape[0]
    return value.reshape(count, -1, 128)


def pick_pair(swapped_here, theirs, ours):
    return tuple(
        (
            jnp.where(swapped_here, other_part, mine_part)
            for other_part, mine_part in zip(theirs, ours)
        )
    )


def activate(up_pre, grad_hidden):
    up_sig = jax.nn.sigmoid(up_pre)
    hidden = (up_pre * up_sig).astype(jnp.bfloat16)
    pairing_part = jnp.sum(hidden.astype(jnp.float32) * grad_hidden, -1)
    grad_pre = (grad_hidden * up_sig * (1.0 + up_pre * (1.0 - up_sig))).astype(jnp.bfloat16)
    return (hidden, pairing_part, grad_pre)


def layer(tokens, routes, logits, cotangent, pair_flags, w_up, w_down):
    devices_ex = lax.axis_size("expert")
    experts = devices_ex // 2
    half_way = experts // 2
    here_index = lax.axis_index("expert")
    slot_here = here_index // 2
    first_core = (here_index % 2) == 0
    tok_rows, top_count = routes.shape
    quarter = tokens.shape[1]
    capacity = max(2, 2 * (3 * tok_rows * top_count // (4 * experts)))
    share = capacity // 2
    lanes = 128
    expert_ids = jnp.arange(experts, dtype=jnp.int32)
    paired = jnp.concatenate([pair_flags, pair_flags]) > 0
    owner_slot = jnp.where(paired, (expert_ids + half_way) % experts, expert_ids)
    swapped_here = paired[slot_here]
    affinity = jax.nn.sigmoid(logits)
    weights = affinity / jnp.sum(affinity, -1, keepdims=True)
    scaled = (weights[:, :, None] * cotangent[:, None, :].astype(jnp.float32)).astype(jnp.bfloat16)
    scaled = scaled.reshape(-1, quarter)
    flat_routes = routes.reshape(-1)
    onehot = (flat_routes[:, None] == expert_ids[None, :]).astype(jnp.int32)
    slot_rank = jnp.sum(jnp.cumsum(onehot, 0) * onehot, 1) - 1
    own_weights = (w_up, w_down)
    shifted = passed_along((w_up, w_down), "expert", devices_ex // 2)
    resident = pick_pair(swapped_here, shifted, own_weights)
    target = owner_slot[flat_routes]
    position = target * capacity + slot_rank
    empty_rows = jnp.zeros((experts * capacity, quarter), jnp.bfloat16)
    token_buf = (
        empty_rows.at[position]
        .set(jnp.repeat(tokens, top_count, axis=0))
        .reshape(experts, capacity, quarter)
    )
    scaled_buf = empty_rows.at[position].set(scaled).reshape(experts, capacity, quarter)
    dispatch = jnp.stack([token_buf, scaled_buf], axis=1).reshape(devices_ex, capacity, quarter)
    got = lax.all_to_all(
        lane_rows(dispatch), "expert", split_axis=0, concat_axis=0, tiled=True
    ).reshape(devices_ex, capacity, quarter)
    partner_got = core_swap(got, "expert")
    routed_rows = jnp.where(first_core, got, partner_got).reshape(-1, quarter)
    scaled_rows = jnp.where(first_core, partner_got, got).reshape(-1, quarter)
    up_block, down_block = resident
    up_part = jnp.dot(routed_rows, up_block, preferred_element_type=jnp.float32)
    grad_part = jnp.dot(scaled_rows, down_block, preferred_element_type=jnp.float32)
    width = up_part.shape[1]
    both = jnp.concatenate(
        [up_part.astype(jnp.bfloat16), grad_part.astype(jnp.bfloat16)], axis=1
    )
    summed = dp_sum(both, "dp").astype(jnp.float32)
    up_pre, grad_hidden = summed[:, :width], summed[:, width:]
    hidden, pairing_part, grad_pre = activate(up_pre, grad_hidden)
    pairing_half = pairing_part.astype(jnp.bfloat16)
    route_half = jnp.einsum(
        "nf,df->nd", grad_pre, up_block, preferred_element_type=jnp.float32
    ).astype(jnp.bfloat16)
    grad_up = jnp.einsum(
        "nd,nf->df", routed_rows, grad_pre, preferred_element_type=jnp.float32
    ).astype(jnp.bfloat16)
    grad_down = jnp.einsum(
        "nd,nf->df", scaled_rows, hidden, preferred_element_type=jnp.float32
    ).astype(jnp.bfloat16)
    lane_ids = jnp.arange(lanes, dtype=jnp.int32)
    my_lane = jnp.where(first_core, 0, 1)
    pair_cols = jnp.where(
        lane_ids[None, None, :] == my_lane,
        pairing_half.reshape(devices_ex, capacity, 1),
        jnp.zeros((), jnp.bfloat16),
    )
    packed = jnp.concatenate(
        [route_half.reshape(devices_ex, capacity, quarter), pair_cols], axis=-1
    )
    low, high = packed[:, :share], packed[:, share:]
    keep = jnp.where(first_core, low, high)
    give = jnp.where(first_core, high, low)
    taken = core_swap(give, "expert")
    combined = (keep.astype(jnp.float32) + taken.astype(jnp.float32)).astype(jnp.bfloat16)
    back = lax.all_to_all(
        lane_rows(combined), "expert", split_axis=0, concat_axis=0, tiled=True
    )
    back_grid = back.reshape(experts, capacity, quarter + lanes)
    picked = back_grid[target, slot_rank]
    grad_tokens = jnp.sum(
        picked[:, :quarter].astype(jnp.float32).reshape(tok_rows, top_count, quarter), 1
    ).astype(jnp.bfloat16)
    pairing_mine = (
        picked[:, quarter].astype(jnp.float32) + picked[:, quarter + 1].astype(jnp.float32)
    ).reshape(tok_rows, top_count)
    grad_logits = (1.0 - affinity) * (
        pairing_mine - weights * jnp.sum(pairing_mine, -1, keepdims=True)
    )
    return (grad_tokens, grad_logits, grad_up, grad_down)


def solution(mesh):
    in_specs = (
        P("expert", "dp"),
        P("expert", None),
        P("expert", None),
        P("expert", "dp"),
        P(),
        P("dp", "expert"),
        P("dp", "expert"),
    )
    out_specs = (P("expert", "dp"), P("expert", None), P("dp", "expert"), P("dp", "expert"))
    return jax.shard_map(layer, mesh=mesh, in_specs=in_specs, out_specs=out_specs, check_vma=False)
```

```python
import jax
import jax.numpy as jnp
from jax import lax
from jax.sharding import PartitionSpec as P


def passed_along(value, axis, steps):
    count = lax.axis_size(axis)
    pairs = [(source, (source + steps) % count) for source in range(count)]
    return lax.ppermute(value, axis, pairs)


def core_swap(value, axis):
    count = lax.axis_size(axis)
    pairs = [(source, source ^ 1) for source in range(count)]
    return lax.ppermute(value, axis, pairs)


def dp_sum(part, axis):
    count = lax.axis_size(axis)
    here = lax.axis_index(axis)
    rows = part.shape[0] // count
    blocks = part.reshape(count, rows, part.shape[1])
    total = blocks[here].astype(jnp.float32)
    for step in range(1, count):
        pairs = [(source, (source + step) % count) for source in range(count)]
        total = total + lax.ppermute(blocks[(here + step) % count], axis, pairs).astype(
            jnp.float32
        )
    reduced = total.astype(jnp.bfloat16)
    gathered = [reduced]
    for step in range(1, count):
        pairs = [(source, (source + step) % count) for source in range(count)]
        gathered.append(lax.ppermute(reduced, axis, pairs))
    stacked = jnp.stack(gathered)
    order = (here - jnp.arange(count)) % count
    return stacked[order].reshape(part.shape)


def lane_rows(value):
    count = value.shape[0]
    return value.reshape(count, -1, 128)


def pick_pair(swapped_here, theirs, ours):
    return tuple(
        (
            jnp.where(swapped_here, other_part, mine_part)
            for other_part, mine_part in zip(theirs, ours)
        )
    )


def activate(up_pre, grad_hidden):
    up_sig = jax.nn.sigmoid(up_pre)
    hidden = (up_pre * up_sig).astype(jnp.bfloat16)
    pairing_part = jnp.sum(hidden.astype(jnp.float32) * grad_hidden, -1)
    grad_pre = (grad_hidden * up_sig * (1.0 + up_pre * (1.0 - up_sig))).astype(jnp.bfloat16)
    return (hidden, pairing_part, grad_pre)


def layer(tokens, routes, logits, cotangent, pair_flags, w_up, w_down):
    devices_ex = lax.axis_size("expert")
    experts = devices_ex // 2
    half_way = experts // 2
    here_index = lax.axis_index("expert")
    slot_here = here_index // 2
    first_core = (here_index % 2) == 0
    tok_rows, top_count = routes.shape
    quarter = tokens.shape[1]
    capacity = max(2, 2 * (3 * tok_rows * top_count // (4 * experts)))
    share = capacity // 2
    lanes = 128
    expert_ids = jnp.arange(experts, dtype=jnp.int32)
    paired = jnp.concatenate([pair_flags, pair_flags]) > 0
    owner_slot = jnp.where(paired, (expert_ids + half_way) % experts, expert_ids)
    swapped_here = paired[slot_here]
    affinity = jax.nn.sigmoid(logits)
    weights = affinity / jnp.sum(affinity, -1, keepdims=True)
    scaled = (weights[:, :, None] * cotangent[:, None, :].astype(jnp.float32)).astype(jnp.bfloat16)
    scaled = scaled.reshape(-1, quarter)
    flat_routes = routes.reshape(-1)
    onehot = (flat_routes[:, None] == expert_ids[None, :]).astype(jnp.int32)
    slot_rank = jnp.sum(jnp.cumsum(onehot, 0) * onehot, 1) - 1
    own_weights = (w_up, w_down)
    shifted = passed_along((w_up, w_down), "expert", devices_ex // 2)
    resident = pick_pair(swapped_here, shifted, own_weights)
    target = owner_slot[flat_routes]
    token_pos = (2 * target * capacity + slot_rank).reshape(tok_rows, top_count)
    scaled_pos = (2 * target + 1) * capacity + slot_rank
    row_ids = jnp.arange(devices_ex * capacity, dtype=jnp.int32)[:, None]
    pick_token = jnp.any(row_ids[:, :, None] == token_pos[None, :, :], -1)
    pick_scaled = row_ids == scaled_pos[None, :]
    picker = jnp.concatenate([pick_token, pick_scaled], axis=1).astype(jnp.bfloat16)
    sources = jnp.concatenate([tokens, scaled], axis=0)
    dispatch = (
        jnp.dot(picker, sources, preferred_element_type=jnp.float32)
        .astype(jnp.bfloat16)
        .reshape(devices_ex, capacity, quarter)
    )
    got = lax.all_to_all(
        lane_rows(dispatch), "expert", split_axis=0, concat_axis=0, tiled=True
    ).reshape(devices_ex, capacity, quarter)
    partner_got = core_swap(got, "expert")
    routed_rows = jnp.where(first_core, got, partner_got).reshape(-1, quarter)
    scaled_rows = jnp.where(first_core, partner_got, got).reshape(-1, quarter)
    up_block, down_block = resident
    up_part = jnp.dot(routed_rows, up_block, preferred_element_type=jnp.float32)
    grad_part = jnp.dot(scaled_rows, down_block, preferred_element_type=jnp.float32)
    width = up_part.shape[1]
    both = jnp.concatenate(
        [up_part.astype(jnp.bfloat16), grad_part.astype(jnp.bfloat16)], axis=1
    )
    summed = dp_sum(both, "dp").astype(jnp.float32)
    up_pre, grad_hidden = summed[:, :width], summed[:, width:]
    hidden, pairing_part, grad_pre = activate(up_pre, grad_hidden)
    pairing_half = pairing_part.astype(jnp.bfloat16)
    route_half = jnp.einsum(
        "nf,df->nd", grad_pre, up_block, preferred_element_type=jnp.float32
    ).astype(jnp.bfloat16)
    grad_up = jnp.einsum(
        "nd,nf->df", routed_rows, grad_pre, preferred_element_type=jnp.float32
    ).astype(jnp.bfloat16)
    grad_down = jnp.einsum(
        "nd,nf->df", scaled_rows, hidden, preferred_element_type=jnp.float32
    ).astype(jnp.bfloat16)
    lane_ids = jnp.arange(lanes, dtype=jnp.int32)
    my_lane = jnp.where(first_core, 0, 1)
    pair_cols = jnp.where(
        lane_ids[None, None, :] == my_lane,
        pairing_half.reshape(devices_ex, capacity, 1),
        jnp.zeros((), jnp.bfloat16),
    )
    packed = jnp.concatenate(
        [route_half.reshape(devices_ex, capacity, quarter), pair_cols], axis=-1
    )
    low, high = packed[:, :share], packed[:, share:]
    keep = jnp.where(first_core, low, high)
    give = jnp.where(first_core, high, low)
    taken = core_swap(give, "expert")
    combined = (keep.astype(jnp.float32) + taken.astype(jnp.float32)).astype(jnp.bfloat16)
    back = lax.all_to_all(
        lane_rows(combined), "expert", split_axis=0, concat_axis=0, tiled=True
    )
    back_rows = back.reshape(experts * capacity, quarter + lanes)
    route_pos = target * capacity + slot_rank
    slot_ids = jnp.arange(experts * capacity, dtype=jnp.int32)[None, :]
    of_route = route_pos[:, None] == slot_ids
    of_token = jnp.any(of_route.reshape(tok_rows, top_count, -1), 1).astype(jnp.bfloat16)
    grad_tokens = jnp.dot(
        of_token, back_rows[:, :quarter], preferred_element_type=jnp.float32
    ).astype(jnp.bfloat16)
    pair_lanes = jnp.dot(
        of_route.astype(jnp.bfloat16), back_rows[:, quarter:], preferred_element_type=jnp.float32
    )
    pairing_mine = (pair_lanes[:, 0] + pair_lanes[:, 1]).reshape(tok_rows, top_count)
    grad_logits = (1.0 - affinity) * (
        pairing_mine - weights * jnp.sum(pairing_mine, -1, keepdims=True)
    )
    return (grad_tokens, grad_logits, grad_up, grad_down)


def solution(mesh):
    in_specs = (
        P("expert", "dp"),
        P("expert", None),
        P("expert", None),
        P("expert", "dp"),
        P(),
        P("dp", "expert"),
        P("dp", "expert"),
    )
    out_specs = (P("expert", "dp"), P("expert", None), P("dp", "expert"), P("dp", "expert"))
    return jax.shard_map(layer, mesh=mesh, in_specs=in_specs, out_specs=out_specs, check_vma=False)
```

```python
import jax
import jax.numpy as jnp
from jax import lax
from jax.sharding import PartitionSpec as P


def passed_along(value, axis, steps):
    count = lax.axis_size(axis)
    pairs = [(source, (source + steps) % count) for source in range(count)]
    return lax.ppermute(value, axis, pairs)


def core_swap(value, axis):
    count = lax.axis_size(axis)
    pairs = [(source, source ^ 1) for source in range(count)]
    return lax.ppermute(value, axis, pairs)


def dp_sum(part, axis):
    count = lax.axis_size(axis)
    here = lax.axis_index(axis)
    rows = part.shape[0] // count
    blocks = part.reshape(count, rows, part.shape[1])
    total = blocks[here].astype(jnp.float32)
    for step in range(1, count):
        pairs = [(source, (source + step) % count) for source in range(count)]
        total = total + lax.ppermute(blocks[(here + step) % count], axis, pairs).astype(
            jnp.float32
        )
    reduced = total.astype(jnp.bfloat16)
    gathered = [reduced]
    for step in range(1, count):
        pairs = [(source, (source + step) % count) for source in range(count)]
        gathered.append(lax.ppermute(reduced, axis, pairs))
    stacked = jnp.stack(gathered)
    order = (here - jnp.arange(count)) % count
    return stacked[order].reshape(part.shape)


def lane_rows(value):
    count = value.shape[0]
    return value.reshape(count, -1, 128)


def pick_pair(swapped_here, theirs, ours):
    return tuple(
        (
            jnp.where(swapped_here, other_part, mine_part)
            for other_part, mine_part in zip(theirs, ours)
        )
    )


def activate(up_pre, grad_hidden):
    up_sig = jax.nn.sigmoid(up_pre)
    hidden = (up_pre * up_sig).astype(jnp.bfloat16)
    pairing_part = jnp.sum(hidden.astype(jnp.float32) * grad_hidden, -1)
    grad_pre = (grad_hidden * up_sig * (1.0 + up_pre * (1.0 - up_sig))).astype(jnp.bfloat16)
    return (hidden, pairing_part, grad_pre)


def layer(tokens, routes, logits, cotangent, pair_flags, w_up, w_down):
    devices_ex = lax.axis_size("expert")
    experts = devices_ex // 2
    half_way = experts // 2
    here_index = lax.axis_index("expert")
    slot_here = here_index // 2
    first_core = (here_index % 2) == 0
    tok_rows, top_count = routes.shape
    quarter = tokens.shape[1]
    capacity = max(2, 2 * (3 * tok_rows * top_count // (4 * experts)))
    share = capacity // 2
    lanes = 128
    expert_ids = jnp.arange(experts, dtype=jnp.int32)
    paired = jnp.concatenate([pair_flags, pair_flags]) > 0
    owner_slot = jnp.where(paired, (expert_ids + half_way) % experts, expert_ids)
    swapped_here = paired[slot_here]
    affinity = jax.nn.sigmoid(logits)
    weights = affinity / jnp.sum(affinity, -1, keepdims=True)
    scaled = (weights[:, :, None] * cotangent[:, None, :].astype(jnp.float32)).astype(jnp.bfloat16)
    scaled = scaled.reshape(-1, quarter)
    flat_routes = routes.reshape(-1)
    onehot = (flat_routes[:, None] == expert_ids[None, :]).astype(jnp.int32)
    slot_rank = jnp.sum(jnp.cumsum(onehot, 0) * onehot, 1) - 1
    own_weights = (w_up, w_down)
    shifted = passed_along((w_up, w_down), "expert", devices_ex // 2)
    resident = pick_pair(swapped_here, shifted, own_weights)
    target = owner_slot[flat_routes]
    token_pos = (2 * target * capacity + slot_rank).reshape(tok_rows, top_count)
    scaled_pos = (2 * target + 1) * capacity + slot_rank
    row_ids = jnp.arange(devices_ex * capacity, dtype=jnp.int32)[:, None]
    pick_token = jnp.any(row_ids[:, :, None] == token_pos[None, :, :], -1)
    pick_scaled = row_ids == scaled_pos[None, :]
    picker = jnp.concatenate([pick_token, pick_scaled], axis=1).astype(jnp.bfloat16)
    sources = jnp.concatenate([tokens, scaled], axis=0)
    dispatch = (
        jnp.dot(picker, sources, preferred_element_type=jnp.float32)
        .astype(jnp.bfloat16)
        .reshape(devices_ex, capacity, quarter)
    )
    got = lax.all_to_all(
        lane_rows(dispatch), "expert", split_axis=0, concat_axis=0, tiled=True
    ).reshape(devices_ex, capacity, quarter)
    partner_got = core_swap(got, "expert")
    routed_rows = jnp.where(first_core, got, partner_got).reshape(-1, quarter)
    scaled_rows = jnp.where(first_core, partner_got, got).reshape(-1, quarter)
    up_block, down_block = resident
    up_part = jnp.dot(routed_rows, up_block, preferred_element_type=jnp.float32)
    grad_part = jnp.dot(scaled_rows, down_block, preferred_element_type=jnp.float32)
    width = up_part.shape[1]
    both = jnp.concatenate(
        [up_part.astype(jnp.bfloat16), grad_part.astype(jnp.bfloat16)], axis=1
    )
    summed = dp_sum(both, "dp").astype(jnp.float32)
    up_pre, grad_hidden = summed[:, :width], summed[:, width:]
    hidden, pairing_part, grad_pre = activate(up_pre, grad_hidden)
    pairing_half = pairing_part.astype(jnp.bfloat16)
    route_half = jnp.einsum(
        "nf,df->nd", grad_pre, up_block, preferred_element_type=jnp.float32
    ).astype(jnp.bfloat16)
    grad_up = jnp.einsum(
        "nd,nf->df", routed_rows, grad_pre, preferred_element_type=jnp.float32
    ).astype(jnp.bfloat16)
    grad_down = jnp.einsum(
        "nd,nf->df", scaled_rows, hidden, preferred_element_type=jnp.float32
    ).astype(jnp.bfloat16)
    lane_ids = jnp.arange(lanes, dtype=jnp.int32)
    my_lane = jnp.where(first_core, 0, 1)
    pair_cols = jnp.where(
        lane_ids[None, None, :] == my_lane,
        pairing_half.reshape(devices_ex, capacity, 1),
        jnp.zeros((), jnp.bfloat16),
    )
    packed = jnp.concatenate(
        [route_half.reshape(devices_ex, capacity, quarter), pair_cols], axis=-1
    )
    low, high = packed[:, :share], packed[:, share:]
    keep = jnp.where(first_core, low, high)
    give = jnp.where(first_core, high, low)
    taken = core_swap(give, "expert")
    combined = (keep.astype(jnp.float32) + taken.astype(jnp.float32)).astype(jnp.bfloat16)
    back = lax.all_to_all(
        lane_rows(combined), "expert", split_axis=0, concat_axis=0, tiled=True
    )
    back_grid = back.reshape(experts, capacity, quarter + lanes)
    picked = back_grid[target, slot_rank]
    grad_tokens = jnp.sum(
        picked[:, :quarter].astype(jnp.float32).reshape(tok_rows, top_count, quarter), 1
    ).astype(jnp.bfloat16)
    pairing_mine = (
        picked[:, quarter].astype(jnp.float32) + picked[:, quarter + 1].astype(jnp.float32)
    ).reshape(tok_rows, top_count)
    grad_logits = (1.0 - affinity) * (
        pairing_mine - weights * jnp.sum(pairing_mine, -1, keepdims=True)
    )
    return (grad_tokens, grad_logits, grad_up, grad_down)


def solution(mesh):
    in_specs = (
        P("expert", "dp"),
        P("expert", None),
        P("expert", None),
        P("expert", "dp"),
        P(),
        P("dp", "expert"),
        P("dp", "expert"),
    )
    out_specs = (P("expert", "dp"), P("expert", None), P("dp", "expert"), P("dp", "expert"))
    return jax.shard_map(layer, mesh=mesh, in_specs=in_specs, out_specs=out_specs, check_vma=False)
```

```python
import jax
import jax.numpy as jnp
from jax import lax
from jax.sharding import PartitionSpec as P


def passed_along(value, axis, steps):
    count = lax.axis_size(axis)
    pairs = [(source, (source + steps) % count) for source in range(count)]
    return lax.ppermute(value, axis, pairs)


def core_swap(value, axis):
    count = lax.axis_size(axis)
    pairs = [(source, source ^ 1) for source in range(count)]
    return lax.ppermute(value, axis, pairs)


def dp_sum(part, axis):
    count = lax.axis_size(axis)
    here = lax.axis_index(axis)
    rows = part.shape[0] // count
    blocks = part.reshape(count, rows, part.shape[1])
    total = blocks[here].astype(jnp.float32)
    for step in range(1, count):
        pairs = [(source, (source + step) % count) for source in range(count)]
        total = total + lax.ppermute(blocks[(here + step) % count], axis, pairs).astype(
            jnp.float32
        )
    reduced = total.astype(jnp.bfloat16)
    gathered = [reduced]
    for step in range(1, count):
        pairs = [(source, (source + step) % count) for source in range(count)]
        gathered.append(lax.ppermute(reduced, axis, pairs))
    stacked = jnp.stack(gathered)
    order = (here - jnp.arange(count)) % count
    return stacked[order].reshape(part.shape)


def lane_rows(value):
    count = value.shape[0]
    return value.reshape(count, -1, 128)


def activate(up_pre, grad_hidden):
    up_sig = jax.nn.sigmoid(up_pre)
    hidden = (up_pre * up_sig).astype(jnp.bfloat16)
    pairing_part = jnp.sum(hidden.astype(jnp.float32) * grad_hidden, -1)
    grad_pre = (grad_hidden * up_sig * (1.0 + up_pre * (1.0 - up_sig))).astype(jnp.bfloat16)
    return (hidden, pairing_part, grad_pre)


def layer(tokens, routes, logits, cotangent, pair_flags, w_up, w_down):
    devices_ex = lax.axis_size("expert")
    experts = devices_ex // 2
    half_way = experts // 2
    here_index = lax.axis_index("expert")
    slot_here = here_index // 2
    first_core = (here_index % 2) == 0
    tok_rows, top_count = routes.shape
    quarter = tokens.shape[1]
    capacity = max(2, 2 * (3 * tok_rows * top_count // (4 * experts)))
    share = capacity // 2
    lanes = 128
    expert_ids = jnp.arange(experts, dtype=jnp.int32)
    paired = jnp.concatenate([pair_flags, pair_flags]) > 0
    owner_slot = jnp.where(paired, (expert_ids + half_way) % experts, expert_ids)
    swapped_here = paired[slot_here]
    affinity = jax.nn.sigmoid(logits)
    weights = affinity / jnp.sum(affinity, -1, keepdims=True)
    scaled = (weights[:, :, None] * cotangent[:, None, :].astype(jnp.float32)).astype(jnp.bfloat16)
    scaled = scaled.reshape(-1, quarter)
    flat_routes = routes.reshape(-1)
    onehot = (flat_routes[:, None] == expert_ids[None, :]).astype(jnp.int32)
    slot_rank = jnp.sum(jnp.cumsum(onehot, 0) * onehot, 1) - 1
    width = w_up.shape[1]
    own_weights = jnp.concatenate([w_up, w_down], axis=1)
    shifted = passed_along(own_weights, "expert", devices_ex // 2)
    resident_both = jnp.where(swapped_here, shifted, own_weights)
    resident = (resident_both[:, :width], resident_both[:, width:])
    target = owner_slot[flat_routes]
    lead = ((2 * target + slot_rank // share) * 2) * share + slot_rank % share
    token_pos = lead.reshape(tok_rows, top_count)
    scaled_pos = lead + share
    row_ids = jnp.arange(devices_ex * capacity, dtype=jnp.int32)[:, None]
    pick_token = jnp.any(row_ids[:, :, None] == token_pos[None, :, :], -1)
    pick_scaled = row_ids == scaled_pos[None, :]
    picker = jnp.concatenate([pick_token, pick_scaled], axis=1).astype(jnp.bfloat16)
    sources = jnp.concatenate([tokens, scaled], axis=0)
    dispatch = (
        jnp.dot(picker, sources, preferred_element_type=jnp.float32)
        .astype(jnp.bfloat16)
        .reshape(devices_ex, capacity, quarter)
    )
    got = lax.all_to_all(
        lane_rows(dispatch), "expert", split_axis=0, concat_axis=0, tiled=True
    ).reshape(devices_ex, 2, share, quarter)
    partner_got = core_swap(got, "expert")
    routed_rows = jnp.stack([got[:, 0], partner_got[:, 0]]).reshape(-1, quarter)
    scaled_rows = jnp.stack([got[:, 1], partner_got[:, 1]]).reshape(-1, quarter)
    up_block, down_block = resident
    up_part = jnp.dot(routed_rows, up_block, preferred_element_type=jnp.float32)
    grad_part = jnp.dot(scaled_rows, down_block, preferred_element_type=jnp.float32)
    width = up_part.shape[1]
    both = jnp.concatenate(
        [up_part.astype(jnp.bfloat16), grad_part.astype(jnp.bfloat16)], axis=1
    )
    summed = dp_sum(both, "dp").astype(jnp.float32)
    up_pre, grad_hidden = summed[:, :width], summed[:, width:]
    hidden, pairing_part, grad_pre = activate(up_pre, grad_hidden)
    pairing_half = pairing_part.astype(jnp.bfloat16)
    route_half = jnp.einsum(
        "nf,df->nd", grad_pre, up_block, preferred_element_type=jnp.float32
    ).astype(jnp.bfloat16)
    grad_up = jnp.einsum(
        "nd,nf->df", routed_rows, grad_pre, preferred_element_type=jnp.float32
    ).astype(jnp.bfloat16)
    grad_down = jnp.einsum(
        "nd,nf->df", scaled_rows, hidden, preferred_element_type=jnp.float32
    ).astype(jnp.bfloat16)
    lane_ids = jnp.arange(lanes, dtype=jnp.int32)
    my_lane = jnp.where(first_core, 0, 1)
    pair_cols = jnp.where(
        lane_ids[None, None, None, :] == my_lane,
        pairing_half.reshape(2, devices_ex, share, 1),
        jnp.zeros((), jnp.bfloat16),
    )
    packed = jnp.concatenate(
        [route_half.reshape(2, devices_ex, share, quarter), pair_cols], axis=-1
    )
    keep, give = packed[0], packed[1]
    taken = core_swap(give, "expert")
    combined = (keep.astype(jnp.float32) + taken.astype(jnp.float32)).astype(jnp.bfloat16)
    back = lax.all_to_all(
        lane_rows(combined), "expert", split_axis=0, concat_axis=0, tiled=True
    )
    back_grid = back.reshape(experts, capacity, quarter + lanes)
    picked = back_grid[target, slot_rank]
    grad_tokens = jnp.sum(
        picked[:, :quarter].astype(jnp.float32).reshape(tok_rows, top_count, quarter), 1
    ).astype(jnp.bfloat16)
    pairing_mine = (
        picked[:, quarter].astype(jnp.float32) + picked[:, quarter + 1].astype(jnp.float32)
    ).reshape(tok_rows, top_count)
    grad_logits = (1.0 - affinity) * (
        pairing_mine - weights * jnp.sum(pairing_mine, -1, keepdims=True)
    )
    return (grad_tokens, grad_logits, grad_up, grad_down)


def solution(mesh):
    in_specs = (
        P("expert", "dp"),
        P("expert", None),
        P("expert", None),
        P("expert", "dp"),
        P(),
        P("dp", "expert"),
        P("dp", "expert"),
    )
    out_specs = (P("expert", "dp"), P("expert", None), P("dp", "expert"), P("dp", "expert"))
    return jax.shard_map(layer, mesh=mesh, in_specs=in_specs, out_specs=out_specs, check_vma=False)
```

```python
import jax
import jax.numpy as jnp
from jax import lax
from jax.sharding import PartitionSpec as P


def passed_along(value, axis, steps):
    count = lax.axis_size(axis)
    pairs = [(source, (source + steps) % count) for source in range(count)]
    return lax.ppermute(value, axis, pairs)


def core_swap(value, axis):
    count = lax.axis_size(axis)
    pairs = [(source, source ^ 1) for source in range(count)]
    return lax.ppermute(value, axis, pairs)


def dp_sum(part, axis):
    count = lax.axis_size(axis)
    here = lax.axis_index(axis)
    rows = part.shape[0] // count
    blocks = part.reshape(count, rows, part.shape[1])
    total = blocks[here].astype(jnp.float32)
    for step in range(1, count):
        pairs = [(source, (source + step) % count) for source in range(count)]
        total = total + lax.ppermute(blocks[(here + step) % count], axis, pairs).astype(
            jnp.float32
        )
    reduced = total.astype(jnp.bfloat16)
    gathered = [reduced]
    for step in range(1, count):
        pairs = [(source, (source + step) % count) for source in range(count)]
        gathered.append(lax.ppermute(reduced, axis, pairs))
    stacked = jnp.stack(gathered)
    order = (here - jnp.arange(count)) % count
    return stacked[order].reshape(part.shape)


def lane_rows(value):
    count = value.shape[0]
    return value.reshape(count, -1, 128)


def activate(up_pre, grad_hidden):
    up_sig = jax.nn.sigmoid(up_pre)
    hidden = (up_pre * up_sig).astype(jnp.bfloat16)
    pairing_part = jnp.sum(hidden.astype(jnp.float32) * grad_hidden, -1)
    grad_pre = (grad_hidden * up_sig * (1.0 + up_pre * (1.0 - up_sig))).astype(jnp.bfloat16)
    return (hidden, pairing_part, grad_pre)


def layer(tokens, routes, logits, cotangent, pair_flags, w_up, w_down):
    devices_ex = lax.axis_size("expert")
    experts = devices_ex // 2
    half_way = experts // 2
    here_index = lax.axis_index("expert")
    slot_here = here_index // 2
    first_core = (here_index % 2) == 0
    tok_rows, top_count = routes.shape
    quarter = tokens.shape[1]
    capacity = max(2, 2 * (3 * tok_rows * top_count // (4 * experts)))
    share = capacity // 2
    lanes = 128
    expert_ids = jnp.arange(experts, dtype=jnp.int32)
    paired = jnp.concatenate([pair_flags, pair_flags]) > 0
    owner_slot = jnp.where(paired, (expert_ids + half_way) % experts, expert_ids)
    swapped_here = paired[slot_here]
    affinity = jax.nn.sigmoid(logits)
    weights = affinity / jnp.sum(affinity, -1, keepdims=True)
    scaled = (weights[:, :, None] * cotangent[:, None, :].astype(jnp.float32)).astype(jnp.bfloat16)
    scaled = scaled.reshape(-1, quarter)
    flat_routes = routes.reshape(-1)
    onehot = (flat_routes[:, None] == expert_ids[None, :]).astype(jnp.int32)
    slot_rank = jnp.sum(jnp.cumsum(onehot, 0) * onehot, 1) - 1
    width = w_up.shape[1]
    own_weights = jnp.concatenate([w_up, w_down], axis=1)
    shifted = passed_along(own_weights, "expert", devices_ex // 2)
    resident = (
        jnp.where(swapped_here, shifted[:, :width], w_up),
        jnp.where(swapped_here, shifted[:, width:], w_down),
    )
    target = owner_slot[flat_routes]
    lead = ((2 * target + slot_rank // share) * 2) * share + slot_rank % share
    token_pos = lead.reshape(tok_rows, top_count)
    scaled_pos = lead + share
    row_ids = jnp.arange(devices_ex * capacity, dtype=jnp.int32)[:, None]
    pick_token = jnp.any(row_ids[:, :, None] == token_pos[None, :, :], -1)
    pick_scaled = row_ids == scaled_pos[None, :]
    picker = jnp.concatenate([pick_token, pick_scaled], axis=1).astype(jnp.bfloat16)
    sources = jnp.concatenate([tokens, scaled], axis=0)
    dispatch = (
        jnp.dot(picker, sources, preferred_element_type=jnp.float32)
        .astype(jnp.bfloat16)
        .reshape(devices_ex, capacity, quarter)
    )
    got = lax.all_to_all(
        lane_rows(dispatch), "expert", split_axis=0, concat_axis=0, tiled=True
    ).reshape(devices_ex, 2, share, quarter)
    partner_got = core_swap(got, "expert")
    routed_rows = jnp.stack([got[:, 0], partner_got[:, 0]]).reshape(-1, quarter)
    scaled_rows = jnp.stack([got[:, 1], partner_got[:, 1]]).reshape(-1, quarter)
    up_block, down_block = resident
    up_part = jnp.dot(routed_rows, up_block, preferred_element_type=jnp.float32)
    grad_part = jnp.dot(scaled_rows, down_block, preferred_element_type=jnp.float32)
    width = up_part.shape[1]
    both = jnp.concatenate(
        [up_part.astype(jnp.bfloat16), grad_part.astype(jnp.bfloat16)], axis=1
    )
    summed = dp_sum(both, "dp").astype(jnp.float32)
    up_pre, grad_hidden = summed[:, :width], summed[:, width:]
    hidden, pairing_part, grad_pre = activate(up_pre, grad_hidden)
    pairing_half = pairing_part.astype(jnp.bfloat16)
    route_half = jnp.einsum(
        "nf,df->nd", grad_pre, up_block, preferred_element_type=jnp.float32
    ).astype(jnp.bfloat16)
    grad_up = jnp.einsum(
        "nd,nf->df", routed_rows, grad_pre, preferred_element_type=jnp.float32
    ).astype(jnp.bfloat16)
    grad_down = jnp.einsum(
        "nd,nf->df", scaled_rows, hidden, preferred_element_type=jnp.float32
    ).astype(jnp.bfloat16)
    lane_ids = jnp.arange(lanes, dtype=jnp.int32)
    my_lane = jnp.where(first_core, 0, 1)
    pair_cols = jnp.where(
        lane_ids[None, None, None, :] == my_lane,
        pairing_half.reshape(2, devices_ex, share, 1),
        jnp.zeros((), jnp.bfloat16),
    )
    packed = jnp.concatenate(
        [route_half.reshape(2, devices_ex, share, quarter), pair_cols], axis=-1
    )
    keep, give = packed[0], packed[1]
    taken = core_swap(give, "expert")
    combined = (keep.astype(jnp.float32) + taken.astype(jnp.float32)).astype(jnp.bfloat16)
    back = lax.all_to_all(
        lane_rows(combined), "expert", split_axis=0, concat_axis=0, tiled=True
    )
    back_grid = back.reshape(experts, capacity, quarter + lanes)
    picked = back_grid[target, slot_rank]
    grad_tokens = jnp.sum(
        picked[:, :quarter].astype(jnp.float32).reshape(tok_rows, top_count, quarter), 1
    ).astype(jnp.bfloat16)
    pairing_mine = (
        picked[:, quarter].astype(jnp.float32) + picked[:, quarter + 1].astype(jnp.float32)
    ).reshape(tok_rows, top_count)
    grad_logits = (1.0 - affinity) * (
        pairing_mine - weights * jnp.sum(pairing_mine, -1, keepdims=True)
    )
    return (grad_tokens, grad_logits, grad_up, grad_down)


def solution(mesh):
    in_specs = (
        P("expert", "dp"),
        P("expert", None),
        P("expert", None),
        P("expert", "dp"),
        P(),
        P("dp", "expert"),
        P("dp", "expert"),
    )
    out_specs = (P("expert", "dp"), P("expert", None), P("dp", "expert"), P("dp", "expert"))
    return jax.shard_map(layer, mesh=mesh, in_specs=in_specs, out_specs=out_specs, check_vma=False)
```

```python
import jax
import jax.numpy as jnp
from jax import lax
from jax.sharding import PartitionSpec as P


def passed_along(value, axis, steps):
    count = lax.axis_size(axis)
    pairs = [(source, (source + steps) % count) for source in range(count)]
    return lax.ppermute(value, axis, pairs)


def core_swap(value, axis):
    count = lax.axis_size(axis)
    pairs = [(source, source ^ 1) for source in range(count)]
    return lax.ppermute(value, axis, pairs)


def dp_sum(part, axis):
    count = lax.axis_size(axis)
    here = lax.axis_index(axis)
    rows = part.shape[0] // count
    blocks = part.reshape(count, rows, part.shape[1])
    total = blocks[here].astype(jnp.float32)
    for step in range(1, count):
        pairs = [(source, (source + step) % count) for source in range(count)]
        total = total + lax.ppermute(blocks[(here + step) % count], axis, pairs).astype(
            jnp.float32
        )
    reduced = total.astype(jnp.bfloat16)
    gathered = [reduced]
    for step in range(1, count):
        pairs = [(source, (source + step) % count) for source in range(count)]
        gathered.append(lax.ppermute(reduced, axis, pairs))
    stacked = jnp.stack(gathered)
    order = (here - jnp.arange(count)) % count
    return stacked[order].reshape(part.shape)


def lane_rows(value):
    count = value.shape[0]
    return value.reshape(count, -1, 128)


def pick_pair(swapped_here, theirs, ours):
    return tuple(
        (
            jnp.where(swapped_here, other_part, mine_part)
            for other_part, mine_part in zip(theirs, ours)
        )
    )


def activate(up_pre, grad_hidden):
    up_sig = jax.nn.sigmoid(up_pre)
    hidden = (up_pre * up_sig).astype(jnp.bfloat16)
    pairing_part = jnp.sum(hidden.astype(jnp.float32) * grad_hidden, -1)
    grad_pre = (grad_hidden * up_sig * (1.0 + up_pre * (1.0 - up_sig))).astype(jnp.bfloat16)
    return (hidden, pairing_part, grad_pre)


def layer(tokens, routes, logits, cotangent, pair_flags, w_up, w_down):
    devices_ex = lax.axis_size("expert")
    experts = devices_ex // 2
    half_way = experts // 2
    here_index = lax.axis_index("expert")
    slot_here = here_index // 2
    first_core = (here_index % 2) == 0
    tok_rows, top_count = routes.shape
    quarter = tokens.shape[1]
    capacity = max(2, 2 * (3 * tok_rows * top_count // (4 * experts)))
    share = capacity // 2
    lanes = 128
    expert_ids = jnp.arange(experts, dtype=jnp.int32)
    paired = jnp.concatenate([pair_flags, pair_flags]) > 0
    owner_slot = jnp.where(paired, (expert_ids + half_way) % experts, expert_ids)
    swapped_here = paired[slot_here]
    affinity = jax.nn.sigmoid(logits)
    weights = affinity / jnp.sum(affinity, -1, keepdims=True)
    scaled = (weights[:, :, None] * cotangent[:, None, :].astype(jnp.float32)).astype(jnp.bfloat16)
    scaled = scaled.reshape(-1, quarter)
    flat_routes = routes.reshape(-1)
    onehot = (flat_routes[:, None] == expert_ids[None, :]).astype(jnp.int32)
    slot_rank = jnp.sum(jnp.cumsum(onehot, 0) * onehot, 1) - 1
    own_weights = (w_up, w_down)
    shifted = passed_along((w_up, w_down), "expert", devices_ex // 2)
    resident = pick_pair(swapped_here, shifted, own_weights)
    target = owner_slot[flat_routes]
    lead = ((2 * target + slot_rank // share) * 2) * share + slot_rank % share
    token_pos = lead.reshape(tok_rows, top_count)
    scaled_pos = lead + share
    row_ids = jnp.arange(devices_ex * capacity, dtype=jnp.int32)[:, None]
    pick_token = jnp.any(row_ids[:, :, None] == token_pos[None, :, :], -1)
    pick_scaled = row_ids == scaled_pos[None, :]
    picker = jnp.concatenate([pick_token, pick_scaled], axis=1).astype(jnp.bfloat16)
    sources = jnp.concatenate([tokens, scaled], axis=0)
    dispatch = (
        jnp.dot(picker, sources, preferred_element_type=jnp.float32)
        .astype(jnp.bfloat16)
        .reshape(devices_ex, capacity, quarter)
    )
    got = lax.all_to_all(
        lane_rows(dispatch), "expert", split_axis=0, concat_axis=0, tiled=True
    ).reshape(devices_ex, 2, share, quarter)
    partner_got = core_swap(got, "expert")
    routed_rows = jnp.stack([got[:, 0], partner_got[:, 0]]).reshape(-1, quarter)
    scaled_rows = jnp.stack([got[:, 1], partner_got[:, 1]]).reshape(-1, quarter)
    up_block, down_block = resident
    up_part = jnp.dot(routed_rows, up_block, preferred_element_type=jnp.float32)
    grad_part = jnp.dot(scaled_rows, down_block, preferred_element_type=jnp.float32)
    width = up_part.shape[1]
    both = jnp.concatenate(
        [up_part.astype(jnp.bfloat16), grad_part.astype(jnp.bfloat16)], axis=1
    )
    summed = dp_sum(both, "dp").astype(jnp.float32)
    up_pre, grad_hidden = summed[:, :width], summed[:, width:]
    hidden, pairing_part, grad_pre = activate(up_pre, grad_hidden)
    pairing_half = pairing_part.astype(jnp.bfloat16)
    route_half = jnp.einsum(
        "nf,df->nd", grad_pre, up_block, preferred_element_type=jnp.float32
    ).astype(jnp.bfloat16)
    grad_up = jnp.einsum(
        "nd,nf->df", routed_rows, grad_pre, preferred_element_type=jnp.float32
    ).astype(jnp.bfloat16)
    grad_down = jnp.einsum(
        "nd,nf->df", scaled_rows, hidden, preferred_element_type=jnp.float32
    ).astype(jnp.bfloat16)
    lane_ids = jnp.arange(lanes, dtype=jnp.int32)
    my_lane = jnp.where(first_core, 0, 1)
    pair_cols = jnp.where(
        lane_ids[None, None, None, :] == my_lane,
        pairing_half.reshape(2, devices_ex, share, 1),
        jnp.zeros((), jnp.bfloat16),
    )
    packed = jnp.concatenate(
        [route_half.reshape(2, devices_ex, share, quarter), pair_cols], axis=-1
    )
    keep, give = packed[0], packed[1]
    taken = core_swap(give, "expert")
    combined = (keep.astype(jnp.float32) + taken.astype(jnp.float32)).astype(jnp.bfloat16)
    back = lax.all_to_all(
        lane_rows(combined), "expert", split_axis=0, concat_axis=0, tiled=True
    )
    back_grid = back.reshape(experts, capacity, quarter + lanes)
    picked = back_grid[target, slot_rank]
    grad_tokens = jnp.sum(
        picked[:, :quarter].astype(jnp.float32).reshape(tok_rows, top_count, quarter), 1
    ).astype(jnp.bfloat16)
    pairing_mine = (
        picked[:, quarter].astype(jnp.float32) + picked[:, quarter + 1].astype(jnp.float32)
    ).reshape(tok_rows, top_count)
    grad_logits = (1.0 - affinity) * (
        pairing_mine - weights * jnp.sum(pairing_mine, -1, keepdims=True)
    )
    return (grad_tokens, grad_logits, grad_up, grad_down)


def solution(mesh):
    in_specs = (
        P("expert", "dp"),
        P("expert", None),
        P("expert", None),
        P("expert", "dp"),
        P(),
        P("dp", "expert"),
        P("dp", "expert"),
    )
    out_specs = (P("expert", "dp"), P("expert", None), P("dp", "expert"), P("dp", "expert"))
    return jax.shard_map(layer, mesh=mesh, in_specs=in_specs, out_specs=out_specs, check_vma=False)
```

```python
import jax
import jax.numpy as jnp
from jax import lax
from jax.sharding import PartitionSpec as P


def passed_along(value, axis, steps):
    count = lax.axis_size(axis)
    pairs = [(source, (source + steps) % count) for source in range(count)]
    return lax.ppermute(value, axis, pairs)


def core_swap(value, axis):
    count = lax.axis_size(axis)
    pairs = [(source, source ^ 1) for source in range(count)]
    return lax.ppermute(value, axis, pairs)


def dp_sum(part, axis):
    count = lax.axis_size(axis)
    here = lax.axis_index(axis)
    rows = part.shape[0] // count
    blocks = part.reshape(count, rows, part.shape[1])
    total = blocks[here].astype(jnp.float32)
    for step in range(1, count):
        pairs = [(source, (source + step) % count) for source in range(count)]
        total = total + lax.ppermute(blocks[(here + step) % count], axis, pairs).astype(
            jnp.float32
        )
    reduced = total.astype(jnp.bfloat16)
    gathered = [reduced]
    for step in range(1, count):
        pairs = [(source, (source + step) % count) for source in range(count)]
        gathered.append(lax.ppermute(reduced, axis, pairs))
    stacked = jnp.stack(gathered)
    order = (here - jnp.arange(count)) % count
    return stacked[order].reshape(part.shape)


def lane_rows(value):
    count = value.shape[0]
    return value.reshape(count, -1, 128)


def activate(up_pre, grad_hidden):
    up_sig = jax.nn.sigmoid(up_pre)
    hidden = (up_pre * up_sig).astype(jnp.bfloat16)
    pairing_part = jnp.sum(hidden.astype(jnp.float32) * grad_hidden, -1)
    grad_pre = (grad_hidden * up_sig * (1.0 + up_pre * (1.0 - up_sig))).astype(jnp.bfloat16)
    return (hidden, pairing_part, grad_pre)


def layer(tokens, routes, logits, cotangent, pair_flags, w_up, w_down):
    devices_ex = lax.axis_size("expert")
    experts = devices_ex // 2
    half_way = experts // 2
    here_index = lax.axis_index("expert")
    slot_here = here_index // 2
    first_core = (here_index % 2) == 0
    tok_rows, top_count = routes.shape
    quarter = tokens.shape[1]
    capacity = max(2, 2 * (3 * tok_rows * top_count // (4 * experts)))
    share = capacity // 2
    lanes = 128
    expert_ids = jnp.arange(experts, dtype=jnp.int32)
    paired = jnp.concatenate([pair_flags, pair_flags]) > 0
    owner_slot = jnp.where(paired, (expert_ids + half_way) % experts, expert_ids)
    swapped_here = paired[slot_here]
    affinity = jax.nn.sigmoid(logits)
    weights = affinity / jnp.sum(affinity, -1, keepdims=True)
    scaled = (weights[:, :, None] * cotangent[:, None, :].astype(jnp.float32)).astype(jnp.bfloat16)
    scaled = scaled.reshape(-1, quarter)
    flat_routes = routes.reshape(-1)
    onehot = (flat_routes[:, None] == expert_ids[None, :]).astype(jnp.int32)
    slot_rank = jnp.sum(jnp.cumsum(onehot, 0) * onehot, 1) - 1
    width = w_up.shape[1]
    own_weights = jnp.concatenate([w_up, w_down], axis=1)
    shifted = passed_along(own_weights, "expert", devices_ex // 2)
    resident_both = jnp.where(swapped_here, shifted, own_weights)
    resident = (resident_both[:, :width], resident_both[:, width:])
    target = owner_slot[flat_routes]
    lead = ((2 * target + slot_rank // share) * 2) * share + slot_rank % share
    token_pos = lead.reshape(tok_rows, top_count)
    scaled_pos = lead + share
    row_ids = jnp.arange(devices_ex * capacity, dtype=jnp.int32)[:, None]
    pick_token = jnp.any(row_ids[:, :, None] == token_pos[None, :, :], -1)
    pick_scaled = row_ids == scaled_pos[None, :]
    picker = jnp.concatenate([pick_token, pick_scaled], axis=1).astype(jnp.bfloat16)
    sources = jnp.concatenate([tokens, scaled], axis=0)
    dispatch = (
        jnp.dot(picker, sources, preferred_element_type=jnp.float32)
        .astype(jnp.bfloat16)
        .reshape(devices_ex, capacity, quarter)
    )
    got = lax.all_to_all(
        lane_rows(dispatch), "expert", split_axis=0, concat_axis=0, tiled=True
    ).reshape(devices_ex, 2, share, quarter)
    partner_got = core_swap(got, "expert")
    routed_rows = jnp.stack([got[:, 0], partner_got[:, 0]]).reshape(-1, quarter)
    scaled_rows = jnp.stack([got[:, 1], partner_got[:, 1]]).reshape(-1, quarter)
    up_block, down_block = resident
    up_part = jnp.dot(routed_rows, up_block, preferred_element_type=jnp.float32)
    grad_part = jnp.dot(scaled_rows, down_block, preferred_element_type=jnp.float32)
    width = up_part.shape[1]
    both = jnp.concatenate(
        [up_part.astype(jnp.bfloat16), grad_part.astype(jnp.bfloat16)], axis=1
    )
    summed = dp_sum(both, "dp")
    up_pre = summed[:, :width].astype(jnp.float32)
    grad_hidden = summed[:, width:].astype(jnp.float32)
    hidden, pairing_part, grad_pre = activate(up_pre, grad_hidden)
    pairing_half = pairing_part.astype(jnp.bfloat16)
    route_half = jnp.einsum(
        "nf,df->nd", grad_pre, up_block, preferred_element_type=jnp.float32
    ).astype(jnp.bfloat16)
    grad_up = jnp.einsum(
        "nd,nf->df", routed_rows, grad_pre, preferred_element_type=jnp.float32
    ).astype(jnp.bfloat16)
    grad_down = jnp.einsum(
        "nd,nf->df", scaled_rows, hidden, preferred_element_type=jnp.float32
    ).astype(jnp.bfloat16)
    lane_ids = jnp.arange(lanes, dtype=jnp.int32)
    my_lane = jnp.where(first_core, 0, 1)
    pair_cols = jnp.where(
        lane_ids[None, None, None, :] == my_lane,
        pairing_half.reshape(2, devices_ex, share, 1),
        jnp.zeros((), jnp.bfloat16),
    )
    packed = jnp.concatenate(
        [route_half.reshape(2, devices_ex, share, quarter), pair_cols], axis=-1
    )
    keep, give = packed[0], packed[1]
    taken = core_swap(give, "expert")
    combined = (keep.astype(jnp.float32) + taken.astype(jnp.float32)).astype(jnp.bfloat16)
    back = lax.all_to_all(
        lane_rows(combined), "expert", split_axis=0, concat_axis=0, tiled=True
    )
    back_grid = back.reshape(experts, capacity, quarter + lanes)
    picked = back_grid[target, slot_rank]
    grad_tokens = jnp.sum(
        picked[:, :quarter].astype(jnp.float32).reshape(tok_rows, top_count, quarter), 1
    ).astype(jnp.bfloat16)
    pairing_mine = (
        picked[:, quarter].astype(jnp.float32) + picked[:, quarter + 1].astype(jnp.float32)
    ).reshape(tok_rows, top_count)
    grad_logits = (1.0 - affinity) * (
        pairing_mine - weights * jnp.sum(pairing_mine, -1, keepdims=True)
    )
    return (grad_tokens, grad_logits, grad_up, grad_down)


def solution(mesh):
    in_specs = (
        P("expert", "dp"),
        P("expert", None),
        P("expert", None),
        P("expert", "dp"),
        P(),
        P("dp", "expert"),
        P("dp", "expert"),
    )
    out_specs = (P("expert", "dp"), P("expert", None), P("dp", "expert"), P("dp", "expert"))
    return jax.shard_map(layer, mesh=mesh, in_specs=in_specs, out_specs=out_specs, check_vma=False)
```
